256 devices in a mesh: tm: 16 (over z, core), pitch: 16 (over y, x).
Axes of the slice: x: 4, y: 4, z: 8, core: 2. Of those that a mesh axis runs over, the one named last changes fastest.
Arguments:
- queries: bfloat16 [128, 512, 2048], P('pitch', 'tm'), may hold values from -30 to 30
- keys: bfloat16 [128, 512, 2048], P('pitch', 'tm'), may hold values from -30 to 30
- values: bfloat16 [128, 512, 2048], P('pitch', 'tm'), may hold values from -6 to 6
- cotangent: bfloat16 [128, 512, 2048], P('pitch', 'tm'), may hold values from -6 to 6
- w_out: bfloat16 [2048, 2048], replicated, may hold values from -0.125 to 0.125
- block_lists: int32 [32, 4], replicated, may hold values from 0 to 31, as said below
- list_counts: int32 [32], replicated, may hold values from 2 to 4, as said below
Outputs:
- block_out: bfloat16 [128, 512, 2048], P('pitch', 'tm')
- grad_queries: bfloat16 [128, 512, 2048], P('pitch', 'tm')
- grad_keys: bfloat16 [128, 512, 2048], P('pitch', 'tm')
- grad_values: bfloat16 [128, 512, 2048], P('pitch', 'tm')
The draws below stay inside these ranges and needn't reach their ends.
Inputs may be any that keep to these rules, and one draw needn't show every extreme that they name: `block_lists`: entry 0 of row b is b; entries 0 to list_counts[b] - 1 are distinct blocks within 2 blocks of b; later entries equal b. `list_counts`: some block uses all 4 entries.
All inputs are finite; a program needn't handle non-finite values.
Results may differ from the reference program's by a relative error of at most 0.034.
Values may be sent and summed in bfloat16 or wider, within the bound.
No kernel may reach another device: no remote copies, remote signals or barrier semaphores. Data moves between devices by JAX's collectives and lax.ppermute only.
A program may use at most 192 MiB of HBM per device.

```python
import math
import jax
import jax.numpy as jnp
from jax import lax

P_SIZE = 128
E = 128
HT = 8
HP = 8
BT = 16
NL = 4
D = 2048
S = 512
NBLK = 32
SPAN = 2


def query_key_pair(key):
    base = jax.random.fold_in(key, 5303)
    shape = (P_SIZE, S, D)
    query_draw = jnp.clip(jax.random.normal(jax.random.fold_in(base, 1), shape, jnp.float32), -6.0, 6.0)
    key_draw = jnp.clip(jax.random.normal(jax.random.fold_in(base, 2), shape, jnp.float32), -6.0, 6.0)
    return (query_draw, key_draw)


def draw_queries(key, part):
    return query_key_pair(key)[0].astype(jnp.bfloat16)


def draw_keys(key, part):
    return query_key_pair(key)[1].astype(jnp.bfloat16)


def list_tables(key):
    base = jax.random.fold_in(key, 7101)
    offsets = jnp.concatenate([jnp.arange(-SPAN, 0), jnp.arange(1, SPAN + 1)]).astype(jnp.int32)
    block_ids = jnp.arange(NBLK, dtype=jnp.int32)[:, None]
    target = block_ids + offsets[None, :]
    inside = (target >= 0) & (target < NBLK)
    order_keys = jax.random.randint(jax.random.fold_in(base, 1), (NBLK, 2 * SPAN), 0, 4096) * (2 * SPAN) + jnp.arange(2 * SPAN, dtype=jnp.int32)[None, :]
    order_keys = jnp.where(inside, order_keys, 4096 * 2 * SPAN + jnp.arange(2 * SPAN, dtype=jnp.int32)[None, :])
    order = jnp.argsort(order_keys, axis=1, stable=True)
    picked = jnp.take_along_axis(target, order[:, :NL - 1], axis=1)
    inside_count = jnp.sum(inside.astype(jnp.int32), axis=1)
    counts = jax.random.randint(jax.random.fold_in(base, 2), (NBLK,), 2, NL + 1)
    counts = jnp.minimum(counts, 1 + inside_count)
    counts = counts.at[NBLK // 2].set(NL)
    tables = jnp.concatenate([block_ids, picked], axis=1)
    used = jnp.arange(NL, dtype=jnp.int32)[None, :] < counts[:, None]
    tables = jnp.where(used, tables, block_ids)
    return (tables.astype(jnp.int32), counts.astype(jnp.int32))


def draw_block_lists(key, part):
    return list_tables(key)[0]


def draw_list_counts(key, part):
    return list_tables(key)[1]


def shard_levels(key, extent, cuts, smallest, high):
    loudness = 1.0
    for dim, parts in cuts:
        draws = jax.random.uniform(jax.random.fold_in(jax.random.fold_in(key, 6), dim), (parts,), jnp.float32, smallest / len(cuts), high / len(cuts))
        loudness = loudness * jnp.repeat(jnp.exp(draws), extent[dim] // parts).reshape((-1,) + (1,) * (len(extent) - 1 - dim))
    return loudness


def bell_draw(rng, shape, spread, bound, cuts=(), kind=jnp.bfloat16):
    result = spread * jax.random.normal(rng, shape, jnp.float32)
    if cuts:
        result = result * shard_levels(rng, shape, cuts, -0.22, 0.18)
    return jnp.clip(result, -bound, bound).astype(kind)


def setup_inputs(seed: int = 0) -> dict:
    seeds = jax.random.split(jax.random.key(seed), 8)
    queries = draw_queries(jax.random.fold_in(seeds[7], 71), 0)
    keys = draw_keys(jax.random.fold_in(seeds[7], 71), 0)
    values = bell_draw(seeds[2], (P_SIZE, S, D), 1.0, 6.0, ((0, 16), (1, 16)))
    cotangent = bell_draw(seeds[3], (P_SIZE, S, D), 1.0, 6.0, ((0, 16), (1, 16)))
    w_out = bell_draw(seeds[4], (D, D), D ** -0.5, 0.125)
    block_lists = draw_block_lists(jax.random.fold_in(seeds[7], 71), 0)
    list_counts = draw_list_counts(jax.random.fold_in(seeds[7], 71), 0)
    return dict(queries=queries, keys=keys, values=values, cotangent=cotangent, w_out=w_out, block_lists=block_lists, list_counts=list_counts)


NEG_FILL = -1e+30

def rounded(array):
    return lax.optimization_barrier(array.astype(jnp.bfloat16)).astype(jnp.float32)

def split_heads(array, start, count):
    return array[..., start:start + count * E].reshape(P_SIZE, S, count, E)

def time_block_scores(query_block, key_sel, usable):
    scale = 1.0 / math.sqrt(E)
    scores = jnp.einsum('pihe,pljhe->philj', query_block.astype(jnp.float32), key_sel.astype(jnp.float32)) * scale
    return jnp.where(usable[None, None, None, :, None], scores, NEG_FILL)

def time_block_forward(query_block, key_sel, value_sel, usable):
    scores = time_block_scores(query_block, key_sel, usable)
    row_max = lax.optimization_barrier(jnp.max(scores, axis=(3, 4), keepdims=True))
    expo = jnp.exp(scores - row_max)
    total = lax.optimization_barrier(jnp.sum(expo, axis=(3, 4), keepdims=True))
    weights = rounded(expo / total)
    output = jnp.einsum('philj,pljhe->pihe', weights, value_sel.astype(jnp.float32))
    return (output, row_max + jnp.log(total))

def time_block_backward(query_block, key_sel, value_sel, usable, grad_block, attn_block, log_total):
    scale = 1.0 / math.sqrt(E)
    scores = time_block_scores(query_block, key_sel, usable)
    back = jnp.exp(scores - log_total)
    dprob = jnp.einsum('pihe,pljhe->philj', grad_block.astype(jnp.float32), value_sel.astype(jnp.float32))
    delta = lax.optimization_barrier(jnp.sum(grad_block.astype(jnp.float32) * attn_block.astype(jnp.float32), axis=-1))
    delta = jnp.transpose(delta, (0, 2, 1))[:, :, :, None, None]
    dscore = rounded(back * (dprob - delta))
    grad_query = jnp.einsum('philj,pljhe->pihe', dscore, key_sel.astype(jnp.float32)) * scale
    grad_key = jnp.einsum('philj,pihe->pljhe', dscore, query_block.astype(jnp.float32)) * scale
    grad_value = jnp.einsum('philj,pihe->pljhe', rounded(back), grad_block.astype(jnp.float32))
    return (grad_query, grad_key, grad_value)

def pitch_stats(query, key):
    scale = 1.0 / math.sqrt(E)
    scores = jnp.einsum('pshe,kshe->shpk', query.astype(jnp.float32), key.astype(jnp.float32)) * scale
    row_max = lax.optimization_barrier(jnp.max(scores, axis=-1, keepdims=True))
    expo = jnp.exp(scores - row_max)
    total = lax.optimization_barrier(jnp.sum(expo, axis=-1, keepdims=True))
    return (scores, row_max, expo, total)

def pitch_forward(query, key, value):
    scores, row_max, expo, total = pitch_stats(query, key)
    return jnp.einsum('shpk,kshe->pshe', rounded(expo / total), value.astype(jnp.float32))

def pitch_backward(query, key, value, grad, attn):
    scale = 1.0 / math.sqrt(E)
    scores, row_max, expo, total = pitch_stats(query, key)
    back = jnp.exp(scores - (row_max + jnp.log(total)))
    dprob = jnp.einsum('pshe,kshe->shpk', grad.astype(jnp.float32), value.astype(jnp.float32))
    delta = jnp.einsum('pshe,pshe->shp', grad.astype(jnp.float32), attn.astype(jnp.float32))[..., None]
    dscore = rounded(back * (dprob - delta))
    grad_query = jnp.einsum('shpk,kshe->pshe', dscore, key.astype(jnp.float32)) * scale
    grad_key = jnp.einsum('shpk,pshe->kshe', dscore, query.astype(jnp.float32)) * scale
    grad_value = jnp.einsum('shpk,pshe->kshe', rounded(back), grad.astype(jnp.float32))
    return (grad_query, grad_key, grad_value)

def reference(queries, keys, values, cotangent, w_out, block_lists, list_counts):
    time_width = HT * E
    q_blocks = queries[..., :time_width].reshape(P_SIZE, NBLK, BT, HT, E)
    k_blocks = keys[..., :time_width].reshape(P_SIZE, NBLK, BT, HT, E)
    v_blocks = values[..., :time_width].reshape(P_SIZE, NBLK, BT, HT, E)
    slot_ids = jnp.arange(NL, dtype=jnp.int32)
    block_ids = jnp.arange(NBLK, dtype=jnp.int32)

    def gather_block(block):
        picked = block_lists[block].astype(jnp.int32)
        usable = slot_ids < list_counts[block]
        query_block = lax.dynamic_index_in_dim(q_blocks, block, 1, keepdims=False)
        return (query_block, jnp.take(k_blocks, picked, axis=1), jnp.take(v_blocks, picked, axis=1), usable, picked)

    def forward_block(block):
        query_block, key_sel, value_sel, usable, picked = gather_block(block)
        return time_block_forward(query_block, key_sel, value_sel, usable)
    time_out, time_log = lax.map(forward_block, block_ids)
    time_out = jnp.moveaxis(time_out, 0, 1).reshape(P_SIZE, S, time_width)
    q_pitch = split_heads(queries, time_width, HP)
    k_pitch = split_heads(keys, time_width, HP)
    v_pitch = split_heads(values, time_width, HP)
    pitch_out = pitch_forward(q_pitch, k_pitch, v_pitch)
    attention = jnp.concatenate([time_out, pitch_out.reshape(P_SIZE, S, HP * E)], axis=-1).astype(jnp.bfloat16)
    block_out = jnp.dot(attention.reshape(P_SIZE * S, D), w_out, preferred_element_type=jnp.float32)
    block_out = block_out.astype(jnp.bfloat16).reshape(P_SIZE, S, D)
    d_attention = lax.dot_general(cotangent.reshape(P_SIZE * S, D), w_out, (((1,), (1,)), ((), ())), preferred_element_type=jnp.float32)
    d_attention = d_attention.astype(jnp.bfloat16).reshape(P_SIZE, S, D)
    grad_blocks = d_attention[..., :time_width].reshape(P_SIZE, NBLK, BT, HT, E)
    attn_blocks = attention[..., :time_width].reshape(P_SIZE, NBLK, BT, HT, E)

    def backward_block(carry, inputs):
        key_acc, value_acc = carry
        block, log_total = inputs
        query_block, key_sel, value_sel, usable, picked = gather_block(block)
        grad_block = lax.dynamic_index_in_dim(grad_blocks, block, 1, keepdims=False)
        attn_block = lax.dynamic_index_in_dim(attn_blocks, block, 1, keepdims=False)
        grad_query, grad_key, grad_value = time_block_backward(query_block, key_sel, value_sel, usable, grad_block, attn_block, log_total)
        return ((key_acc.at[:, picked].add(grad_key), value_acc.at[:, picked].add(grad_value)), grad_query)
    empty = jnp.zeros((P_SIZE, NBLK, BT, HT, E), jnp.float32)
    (key_acc, value_acc), grad_query_time = lax.scan(backward_block, (empty, empty), (block_ids, time_log))
    grad_query_time = jnp.moveaxis(grad_query_time, 0, 1).reshape(P_SIZE, S, time_width)
    pitch_grads = pitch_backward(q_pitch, k_pitch, v_pitch, split_heads(d_attention, time_width, HP), split_heads(attention, time_width, HP))
    grad_queries = jnp.concatenate([grad_query_time, pitch_grads[0].reshape(P_SIZE, S, HP * E)], axis=-1).astype(jnp.bfloat16)
    grad_keys = jnp.concatenate([key_acc.reshape(P_SIZE, S, time_width), pitch_grads[1].reshape(P_SIZE, S, HP * E)], axis=-1).astype(jnp.bfloat16)
    grad_values = jnp.concatenate([value_acc.reshape(P_SIZE, S, time_width), pitch_grads[2].reshape(P_SIZE, S, HP * E)], axis=-1).astype(jnp.bfloat16)
    return (block_out, grad_queries, grad_keys, grad_values)
```

```python
import math

import jax
import jax.numpy as jnp
from jax import lax
from jax.sharding import PartitionSpec as P

E = 128
HT = 8
HP = 8
BT = 16
NL = 4


NEG_FILL = -1e30


def shift(value, axis, by):
    peers = lax.axis_size(axis)
    pairs = [(i, i + by) for i in range(peers) if 0 <= i + by < peers]
    return lax.ppermute(value, axis, pairs)


def attend(query, key, value, grad, mask, scale, qspec, kspec):
    sspec = "bhqk"
    f32 = jnp.float32
    scores = jnp.einsum(f"{qspec},{kspec}->{sspec}", query, key, preferred_element_type=f32)
    scores = scores * scale
    if mask is not None:
        scores = jnp.where(mask, scores, NEG_FILL)
    row_max = jnp.max(scores, axis=-1, keepdims=True)
    expo = jnp.exp(scores - row_max)
    total = jnp.sum(expo, axis=-1, keepdims=True)
    weights = (expo / total).astype(jnp.bfloat16)
    out = jnp.einsum(f"{sspec},{kspec}->{qspec}", weights, value, preferred_element_type=f32)
    out16 = out.astype(jnp.bfloat16)
    log_total = row_max + jnp.log(total)
    back = jnp.exp(scores - log_total)
    dprob = jnp.einsum(f"{qspec},{kspec}->{sspec}", grad, value, preferred_element_type=f32)
    delta = jnp.einsum(f"{qspec},{qspec}->bhq", grad, out16, preferred_element_type=f32)
    dscore = (back * (dprob - delta[..., None])).astype(jnp.bfloat16)
    grad_query = jnp.einsum(f"{sspec},{kspec}->{qspec}", dscore, key, preferred_element_type=f32)
    grad_key = jnp.einsum(f"{sspec},{qspec}->{kspec}", dscore, query, preferred_element_type=f32)
    grad_value = jnp.einsum(
        f"{sspec},{qspec}->{kspec}", back.astype(jnp.bfloat16), grad, preferred_element_type=f32
    )
    return out16, grad_query * scale, grad_key * scale, grad_value


def local(queries, keys, values, cotangent, w_out, block_lists, list_counts):
    rows_pitch, rows_time, width = queries.shape
    spread = rows_time // BT
    time_width = HT * E
    scale = 1.0 / math.sqrt(E)
    bf16 = jnp.bfloat16

    d_attention = lax.dot_general(
        cotangent.reshape(rows_pitch * rows_time, width),
        w_out,
        (((1,), (1,)), ((), ())),
        preferred_element_type=jnp.float32,
    )
    d_attention = d_attention.astype(bf16).reshape(queries.shape)

    def pitch_part(x):
        return x[..., time_width:].reshape(rows_pitch, rows_time, HP, E)

    sent = jnp.stack([pitch_part(queries), pitch_part(keys), pitch_part(values), pitch_part(d_attention)])
    got = lax.all_to_all(sent, "pitch", split_axis=2, concat_axis=1, tiled=True)
    p_out, p_gq, p_gk, p_gv = attend(
        got[0], got[1], got[2], got[3], None, scale, "qbhe", "kbhe"
    )
    back = jnp.stack([p_out, p_gq.astype(bf16), p_gk.astype(bf16), p_gv.astype(bf16)])
    returned = lax.all_to_all(back, "pitch", split_axis=1, concat_axis=2, tiled=True)
    returned = returned.reshape(4, rows_pitch, rows_time, HP * E)

    me = lax.axis_index("tm")
    first_block = me * spread
    kv_own = jnp.stack([keys[..., :time_width], values[..., :time_width]])
    kv_wide = jnp.concatenate([shift(kv_own, "tm", 1), kv_own, shift(kv_own, "tm", -1)], axis=2)
    my_lists = lax.dynamic_slice_in_dim(block_lists, first_block, spread, 0)
    my_counts = lax.dynamic_slice_in_dim(list_counts, first_block, spread, 0)
    used = jnp.arange(NL, dtype=jnp.int32)[None, :] < my_counts[:, None]
    slots = first_block - spread + jnp.arange(3 * spread, dtype=jnp.int32)
    allowed = jnp.any(used[:, :, None] & (my_lists[:, :, None] == slots[None, None, :]), axis=1)
    mask = jnp.repeat(jnp.repeat(allowed, BT, axis=0), BT, axis=1)[None, None]

    def heads(x):
        return x.reshape(x.shape[0], x.shape[1], HT, E)

    t_out, t_gq, t_gk, t_gv = attend(
        heads(queries[..., :time_width]),
        heads(kv_wide[0]),
        heads(kv_wide[1]),
        heads(d_attention[..., :time_width]),
        mask,
        scale,
        "bqhe",
        "bkhe",
    )
    g_wide = jnp.stack([t_gk, t_gv]).reshape(2, rows_pitch, 3 * rows_time, time_width)
    from_next = shift(g_wide[:, :, :rows_time].astype(bf16), "tm", -1)
    from_prev = shift(g_wide[:, :, 2 * rows_time :].astype(bf16), "tm", 1)
    g_own = (
        g_wide[:, :, rows_time : 2 * rows_time]
        + from_next.astype(jnp.float32)
        + from_prev.astype(jnp.float32)
    )

    attention = jnp.concatenate([t_out.reshape(rows_pitch, rows_time, time_width), returned[0]], axis=-1)
    block_out = (
        jnp.dot(attention.reshape(rows_pitch * rows_time, width), w_out, preferred_element_type=jnp.float32)
        .astype(bf16)
        .reshape(queries.shape)
    )
    grad_queries = jnp.concatenate(
        [t_gq.reshape(rows_pitch, rows_time, time_width).astype(bf16), returned[1]], axis=-1
    )
    grad_keys = jnp.concatenate([g_own[0].astype(bf16), returned[2]], axis=-1)
    grad_values = jnp.concatenate([g_own[1].astype(bf16), returned[3]], axis=-1)
    return (block_out, grad_queries, grad_keys, grad_values)


def solution(mesh):
    return jax.shard_map(
        local,
        mesh=mesh,
        in_specs=(
            P("pitch", "tm", None),
            P("pitch", "tm", None),
            P("pitch", "tm", None),
            P("pitch", "tm", None),
            P(),
            P(),
            P(),
        ),
        out_specs=(
            P("pitch", "tm", None),
            P("pitch", "tm", None),
            P("pitch", "tm", None),
            P("pitch", "tm", None),
        ),
        check_vma=False,
    )
```
